32 devices in a mesh: shard: 8 (over z, x), tensor: 4 (over y, core).
Axes of the slice: x: 2, y: 2, z: 4, core: 2. Of those that a mesh axis runs over, the one named last changes fastest.
Arguments:
- wide_weight: bfloat16 [4, 4096, 4096], P(None, 'shard', 'tensor'), may hold values from -6 to 6
- wide_grad: bfloat16 [4, 4096, 4096], P(None, 'shard', 'tensor'), may hold values from -6 to 6
- wide_first: float32 [4, 4096, 256], P(None, ('shard', 'tensor')), may hold values from -4 to 4
- wide_second: float32 [4, 4096, 256], P(None, ('shard', 'tensor')), may hold values from 0.001 to 0.1
- wide_basis: bfloat16 [4, 4096, 256], P(None, 'tensor'), may hold values from -0.09375 to 0.09375
- narrow_weight: bfloat16 [4, 1024, 4096], P(None, 'shard', 'tensor'), may hold values from -6 to 6
- narrow_grad: bfloat16 [4, 1024, 4096], P(None, 'shard', 'tensor'), may hold values from -6 to 6
- narrow_first: float32 [4, 1024, 256], P(None, ('shard', 'tensor')), may hold values from -4 to 4
- narrow_second: float32 [4, 1024, 256], P(None, ('shard', 'tensor')), may hold values from 0.001 to 0.1
- narrow_basis: bfloat16 [4, 4096, 256], P(None, 'tensor'), may hold values from -0.09375 to 0.09375
- vocab_weight: bfloat16 [2, 32000, 4096], P(None, 'shard', 'tensor'), may hold values from -6 to 6
- vocab_grad: bfloat16 [2, 32000, 4096], P(None, 'shard', 'tensor'), may hold values from -6 to 6
- vocab_first: float32 [2, 32000, 256], P(None, ('shard', 'tensor')), may hold values from -4 to 4
- vocab_second: float32 [2, 32000, 256], P(None, ('shard', 'tensor')), may hold values from 0.001 to 0.1
- vocab_basis: bfloat16 [2, 4096, 256], P(None, 'tensor'), may hold values from -0.09375 to 0.09375
Outputs:
- wide_weight_new: bfloat16 [4, 4096, 4096], P(None, 'shard', 'tensor')
- wide_first_new: float32 [4, 4096, 256], P(None, ('shard', 'tensor'))
- wide_second_new: float32 [4, 4096, 256], P(None, ('shard', 'tensor'))
- narrow_weight_new: bfloat16 [4, 1024, 4096], P(None, 'shard', 'tensor')
- narrow_first_new: float32 [4, 1024, 256], P(None, ('shard', 'tensor'))
- narrow_second_new: float32 [4, 1024, 256], P(None, ('shard', 'tensor'))
- vocab_weight_new: bfloat16 [2, 32000, 4096], P(None, 'shard', 'tensor')
- vocab_first_new: float32 [2, 32000, 256], P(None, ('shard', 'tensor'))
- vocab_second_new: float32 [2, 32000, 256], P(None, ('shard', 'tensor'))
The draws below stay inside these ranges and needn't reach their ends.
All inputs are finite; a program needn't handle non-finite values.
Results may differ from the reference program's by a relative error of at most 0.01.
Values may be sent and summed in bfloat16 or wider, within the bound.
No kernel may reach another device: no remote copies, remote signals or barrier semaphores. Data moves between devices by JAX's collectives and lax.ppermute only.
A program may use at most 192 MiB of HBM per device.

```python
import math
import jax
import jax.numpy as jnp
from jax import lax

D = 4096
KV = 1024
VOCAB = 32000
RANK = 256
LAYERS = 2
NS_ITERS = 3
N_TENSOR = 4


def shard_levels(rng, dims, split, least, high):
    factor_of = 1.0
    for dim, parts in split:
        heights = jax.random.uniform(jax.random.fold_in(jax.random.fold_in(rng, 6), dim), (parts,), jnp.float32, least / len(split), high / len(split))
        factor_of = factor_of * jnp.repeat(jnp.exp(heights), dims[dim] // parts).reshape((-1,) + (1,) * (len(dims) - 1 - dim))
    return factor_of


def bell_draw(key, extent, scale, reach, split=(), held_as=jnp.bfloat16):
    drawn = jax.random.normal(key, extent, jnp.float32) * scale
    if len(split) > 0:
        drawn = shard_levels(key, extent, split, -0.22, 0.18) * drawn
    return jnp.clip(drawn, min=-reach, max=reach).astype(held_as)


def setup_inputs(seed: int = 0) -> dict:
    seeds = jax.random.split(jax.random.key(seed), 16)
    return {
        "wide_weight": bell_draw(seeds[0], (2 * LAYERS, D, D), 1.0, 6.0, ((1, 8), (2, 4))),
        "wide_grad": bell_draw(seeds[1], (2 * LAYERS, D, D), 1.0, 6.0, ((1, 8), (2, 4))),
        "wide_first": bell_draw(seeds[2], (2 * LAYERS, D, RANK), 0.3, 4.0, ((1, 32),), jnp.float32),
        "wide_second": jnp.clip(jnp.exp(math.log(0.1) - 4.6051702 * jax.random.uniform(seeds[3], (2 * LAYERS, D, RANK), jnp.float32) ** shard_levels(seeds[3], (2 * LAYERS, D, RANK), ((1, 32),), -0.2, 0.2)), 0.001, 0.1),
        "wide_basis": bell_draw(seeds[4], (2 * LAYERS, D, RANK), D ** -0.5, 0.09375, ((1, 4),)),
        "narrow_weight": bell_draw(seeds[5], (2 * LAYERS, KV, D), 1.0, 6.0, ((1, 8), (2, 4))),
        "narrow_grad": bell_draw(seeds[6], (2 * LAYERS, KV, D), 1.0, 6.0, ((1, 8), (2, 4))),
        "narrow_first": bell_draw(seeds[7], (2 * LAYERS, KV, RANK), 0.3, 4.0, ((1, 32),), jnp.float32),
        "narrow_second": jnp.clip(jnp.exp(math.log(0.1) - 4.6051702 * jax.random.uniform(seeds[8], (2 * LAYERS, KV, RANK), jnp.float32) ** shard_levels(seeds[8], (2 * LAYERS, KV, RANK), ((1, 32),), -0.2, 0.2)), 0.001, 0.1),
        "narrow_basis": bell_draw(seeds[9], (2 * LAYERS, D, RANK), D ** -0.5, 0.09375, ((1, 4),)),
        "vocab_weight": bell_draw(seeds[10], (2, VOCAB, D), 1.0, 6.0, ((1, 8), (2, 4))),
        "vocab_grad": bell_draw(seeds[11], (2, VOCAB, D), 1.0, 6.0, ((1, 8), (2, 4))),
        "vocab_first": bell_draw(seeds[12], (2, VOCAB, RANK), 0.3, 4.0, ((1, 32),), jnp.float32),
        "vocab_second": jnp.clip(jnp.exp(math.log(0.1) - 4.6051702 * jax.random.uniform(seeds[13], (2, VOCAB, RANK), jnp.float32) ** shard_levels(seeds[13], (2, VOCAB, RANK), ((1, 32),), -0.2, 0.2)), 0.001, 0.1),
        "vocab_basis": bell_draw(seeds[14], (2, D, RANK), D ** -0.5, 0.09375, ((1, 4),)),
    }


HIGHEST = lax.Precision.HIGHEST

def refresh_group(weight, grad, first, second, basis):
    count, rows, width = grad.shape
    rank = basis.shape[2]
    cols = width // N_TENSOR
    grad_wide = grad.astype(jnp.float32)
    blocks = jnp.einsum('smjc,sjcr->smjr', grad_wide.reshape(count, rows, N_TENSOR, cols), basis.astype(jnp.float32).reshape(count, N_TENSOR, cols, rank))
    sketch = lax.optimization_barrier(jnp.sum(blocks.astype(jnp.bfloat16).astype(jnp.float32), axis=2)).astype(jnp.bfloat16)
    back = jnp.einsum('smc,smr->scr', grad_wide, sketch.astype(jnp.float32))
    gram = jnp.einsum('sdk,sdl->skl', back, back, precision=HIGHEST)
    trace = jnp.einsum('skk->s', gram)
    scale = 1.0 / jnp.sqrt(trace + 1e-06)
    polish = back * scale[:, None, None]
    gram = gram * (scale * scale)[:, None, None]
    for step in range(NS_ITERS):
        square = jnp.einsum('skl,slm->skm', gram, gram, precision=HIGHEST)
        poly = -4.775 * gram + 2.0315 * square
        polish = 3.4445 * polish + jnp.einsum('sdk,skl->sdl', polish, poly, precision=HIGHEST)
        if step + 1 < NS_ITERS:
            gram = jnp.einsum('sdk,sdl->skl', polish, polish, precision=HIGHEST)
    new_basis = polish.astype(jnp.bfloat16).astype(jnp.float32)
    projected = jnp.einsum('smd,sdr->smr', grad_wide, new_basis)
    first_new = 0.9 * first + 0.1 * projected
    second_new = 0.999 * second + 0.001 * projected * projected
    direction = first_new / (1.0 - 0.9 ** 10) / (jnp.sqrt(second_new / (1.0 - 0.999 ** 10)) + 1e-08)
    direction = direction.astype(jnp.bfloat16).astype(jnp.float32)
    update = jnp.einsum('smr,sdr->smd', direction, new_basis)
    weight_new = (0.99 * weight.astype(jnp.float32) - 2.0 * update).astype(jnp.bfloat16)
    return (weight_new, first_new, second_new)

def reference(wide_weight, wide_grad, wide_first, wide_second, wide_basis, narrow_weight, narrow_grad, narrow_first, narrow_second, narrow_basis, vocab_weight, vocab_grad, vocab_first, vocab_second, vocab_basis):
    wide_out = refresh_group(wide_weight, wide_grad, wide_first, wide_second, wide_basis)
    narrow_out = refresh_group(narrow_weight, narrow_grad, narrow_first, narrow_second, narrow_basis)
    vocab_out = refresh_group(vocab_weight, vocab_grad, vocab_first, vocab_second, vocab_basis)
    return (wide_out[0], wide_out[1], wide_out[2], narrow_out[0], narrow_out[1], narrow_out[2], vocab_out[0], vocab_out[1], vocab_out[2])
```

```python
import functools

import jax
import jax.numpy as jnp
from jax import lax
from jax.sharding import PartitionSpec as P

NS_ITERS = 3


HIGHEST = lax.Precision.HIGHEST


def local_gram(polish):
    return jnp.einsum("sdk,sdl->skl", polish, polish, precision=HIGHEST)


def polish_small(back, gram):
    trace = jnp.einsum("skk->s", gram)
    scale = 1.0 / jnp.sqrt(trace + 1e-06)
    small = gram * (scale * scale)[:, None, None]
    rank = gram.shape[1]
    eye = jnp.eye(rank, dtype=jnp.float32)[None, :, :]
    factor = jnp.broadcast_to(eye, gram.shape)
    for step in range(NS_ITERS):
        square = jnp.einsum("skl,slm->skm", small, small, precision=HIGHEST)
        turn = 3.4445 * eye - 4.775 * small + 2.0315 * square
        factor = jnp.einsum("skl,slm->skm", factor, turn, precision=HIGHEST)
        if step + 1 < NS_ITERS:
            small = jnp.einsum(
                "skl,slm->skm",
                turn,
                jnp.einsum("skl,slm->skm", small, turn, precision=HIGHEST),
                precision=HIGHEST,
            )
    return jnp.einsum("sdk,skl->sdl", back * scale[:, None, None], factor, precision=HIGHEST)


def adam_moments(first, second, projected):
    first_new = 0.9 * first + 0.1 * projected
    second_new = 0.999 * second + 0.001 * projected * projected
    direction = first_new / (1.0 - 0.9**10) / (jnp.sqrt(second_new / (1.0 - 0.999**10)) + 1e-08)
    return (first_new, second_new, direction.astype(jnp.bfloat16))


def split_rows(flat, shapes):
    parts = []
    offset = 0
    for shape in shapes:
        size = 1
        for dim in shape:
            size *= dim
        parts.append(flat[..., offset:offset + size].reshape(flat.shape[:-1] + shape))
        offset += size
    return parts


def per_device(
    tensor_size,
    wide_weight,
    wide_grad,
    wide_first,
    wide_second,
    wide_basis,
    narrow_weight,
    narrow_grad,
    narrow_first,
    narrow_second,
    narrow_basis,
    vocab_weight,
    vocab_grad,
    vocab_first,
    vocab_second,
    vocab_basis,
):
    weights = (wide_weight, narrow_weight, vocab_weight)
    grads = (wide_grad, narrow_grad, vocab_grad)
    firsts = (wide_first, narrow_first, vocab_first)
    seconds = (wide_second, narrow_second, vocab_second)
    olds = (wide_basis, narrow_basis, vocab_basis)
    counts = [grad.shape[0] for grad in grads]
    sketch_terms = [
        jnp.einsum("smc,scr->smr", grad, old, preferred_element_type=jnp.float32).astype(jnp.bfloat16)
        for grad, old in zip(grads, olds)
    ]
    sketches = lax.psum(tuple(sketch_terms), "tensor")
    back_terms = [
        jnp.einsum("smc,smr->scr", grad, sketch, preferred_element_type=jnp.float32)
        for grad, sketch in zip(grads, sketches)
    ]
    back_all = jnp.concatenate(back_terms, axis=0).astype(jnp.bfloat16)
    backs = lax.psum_scatter(back_all, "shard", scatter_dimension=1, tiled=True).astype(jnp.float32)
    grams = lax.psum(local_gram(backs), ("shard", "tensor"))
    rounded = polish_small(backs, grams).astype(jnp.bfloat16)
    basis_all = lax.all_gather(rounded, "shard", axis=1, tiled=True)
    bases = []
    offset = 0
    for count in counts:
        bases.append(basis_all[offset:offset + count])
        offset += count
    proj_parts = []
    row_shapes = []
    for grad, basis in zip(grads, bases):
        count, rows, cols = grad.shape
        split = grad.reshape(count, tensor_size, rows // tensor_size, cols)
        proj = jnp.einsum("sjmc,scr->jsmr", split, basis, preferred_element_type=jnp.float32)
        row_shapes.append((count, rows // tensor_size, basis.shape[2]))
        proj_parts.append(proj.reshape(tensor_size, -1, basis.shape[2]).astype(jnp.bfloat16))
    proj_all = jnp.concatenate(proj_parts, axis=1)
    proj_mine = lax.psum_scatter(proj_all, "tensor", scatter_dimension=0, tiled=True).reshape(-1)
    projected = [part.astype(jnp.float32) for part in split_rows(proj_mine, row_shapes)]
    results = [
        adam_moments(first, second, proj) for first, second, proj in zip(firsts, seconds, projected)
    ]
    dir_all = jnp.concatenate([result[2].reshape(-1) for result in results])
    dir_gathered = lax.all_gather(dir_all, "tensor", axis=0, tiled=False)
    directions = split_rows(dir_gathered, row_shapes)
    outputs = []
    for weight, direction, basis, result in zip(weights, directions, bases, results):
        count, rows, cols = weight.shape
        update = jnp.einsum("jsmr,scr->sjmc", direction, basis, preferred_element_type=jnp.float32)
        update = update.reshape(count, rows, cols)
        weight_new = (0.99 * weight.astype(jnp.float32) - 2.0 * update).astype(jnp.bfloat16)
        outputs.append((weight_new, result[0], result[1]))
    return (
        outputs[0][0],
        outputs[0][1],
        outputs[0][2],
        outputs[1][0],
        outputs[1][1],
        outputs[1][2],
        outputs[2][0],
        outputs[2][1],
        outputs[2][2],
    )


def solution(mesh):
    in_specs = (
        P(None, "shard", "tensor"),
        P(None, "shard", "tensor"),
        P(None, ("shard", "tensor"), None),
        P(None, ("shard", "tensor"), None),
        P(None, "tensor", None),
        P(None, "shard", "tensor"),
        P(None, "shard", "tensor"),
        P(None, ("shard", "tensor"), None),
        P(None, ("shard", "tensor"), None),
        P(None, "tensor", None),
        P(None, "shard", "tensor"),
        P(None, "shard", "tensor"),
        P(None, ("shard", "tensor"), None),
        P(None, ("shard", "tensor"), None),
        P(None, "tensor", None),
    )
    out_specs = (
        P(None, "shard", "tensor"),
        P(None, ("shard", "tensor"), None),
        P(None, ("shard", "tensor"), None),
        P(None, "shard", "tensor"),
        P(None, ("shard", "tensor"), None),
        P(None, ("shard", "tensor"), None),
        P(None, "shard", "tensor"),
        P(None, ("shard", "tensor"), None),
        P(None, ("shard", "tensor"), None),
    )
    return jax.shard_map(
        functools.partial(per_device, mesh.shape["tensor"]), mesh=mesh, in_specs=in_specs, out_specs=out_specs, check_vma=False
    )
```

```python
import functools

import jax
import jax.numpy as jnp
from jax import lax
from jax.sharding import PartitionSpec as P

NS_ITERS = 3


HIGHEST = lax.Precision.HIGHEST


def local_gram(polish):
    return jnp.einsum("sdk,sdl->skl", polish, polish, precision=HIGHEST)


def polish_small(back, gram):
    trace = jnp.einsum("skk->s", gram)
    scale = 1.0 / jnp.sqrt(trace + 1e-06)
    small = gram * (scale * scale)[:, None, None]
    rank = gram.shape[1]
    eye = jnp.eye(rank, dtype=jnp.float32)[None, :, :]
    factor = jnp.broadcast_to(eye, gram.shape)
    for step in range(NS_ITERS):
        square = jnp.einsum("skl,slm->skm", small, small, precision=HIGHEST)
        turn = 3.4445 * eye - 4.775 * small + 2.0315 * square
        factor = jnp.einsum("skl,slm->skm", factor, turn, precision=HIGHEST)
        if step + 1 < NS_ITERS:
            small = jnp.einsum(
                "skl,slm->skm",
                turn,
                jnp.einsum("skl,slm->skm", small, turn, precision=HIGHEST),
                precision=HIGHEST,
            )
    return jnp.einsum("sdk,skl->sdl", back * scale[:, None, None], factor, precision=HIGHEST)


def adam_moments(first, second, projected):
    first_new = 0.9 * first + 0.1 * projected
    second_new = 0.999 * second + 0.001 * projected * projected
    direction = first_new / (1.0 - 0.9**10) / (jnp.sqrt(second_new / (1.0 - 0.999**10)) + 1e-08)
    return (first_new, second_new, direction.astype(jnp.bfloat16))


def split_rows(flat, shapes):
    parts = []
    offset = 0
    for shape in shapes:
        size = 1
        for dim in shape:
            size *= dim
        parts.append(flat[..., offset:offset + size].reshape(flat.shape[:-1] + shape))
        offset += size
    return parts


def per_device(
    tensor_size,
    wide_weight,
    wide_grad,
    wide_first,
    wide_second,
    wide_basis,
    narrow_weight,
    narrow_grad,
    narrow_first,
    narrow_second,
    narrow_basis,
    vocab_weight,
    vocab_grad,
    vocab_first,
    vocab_second,
    vocab_basis,
):
    weights = (wide_weight, narrow_weight, vocab_weight)
    grads = (wide_grad, narrow_grad, vocab_grad)
    firsts = (wide_first, narrow_first, vocab_first)
    seconds = (wide_second, narrow_second, vocab_second)
    olds = (wide_basis, narrow_basis, vocab_basis)
    counts = [grad.shape[0] for grad in grads]
    sketch_terms = [
        jnp.einsum("smc,scr->smr", grad, old, preferred_element_type=jnp.float32).astype(jnp.bfloat16)
        for grad, old in zip(grads, olds)
    ]
    sketches = lax.psum(tuple(sketch_terms), "tensor")
    back_terms = [
        jnp.einsum("smc,smr->scr", grad, sketch, preferred_element_type=jnp.float32)
        for grad, sketch in zip(grads, sketches)
    ]
    back_all = jnp.concatenate(back_terms, axis=0).astype(jnp.bfloat16)
    backs = lax.psum(back_all, "shard").astype(jnp.float32)
    grams = lax.psum(local_gram(backs), "tensor")
    basis_all = polish_small(backs, grams).astype(jnp.bfloat16)
    bases = []
    offset = 0
    for count in counts:
        bases.append(basis_all[offset:offset + count])
        offset += count
    proj_parts = []
    row_shapes = []
    for grad, basis in zip(grads, bases):
        count, rows, cols = grad.shape
        split = grad.reshape(count, tensor_size, rows // tensor_size, cols)
        proj = jnp.einsum("sjmc,scr->jsmr", split, basis, preferred_element_type=jnp.float32)
        row_shapes.append((count, rows // tensor_size, basis.shape[2]))
        proj_parts.append(proj.reshape(tensor_size, -1, basis.shape[2]).astype(jnp.bfloat16))
    proj_all = jnp.concatenate(proj_parts, axis=1)
    proj_mine = lax.psum_scatter(proj_all, "tensor", scatter_dimension=0, tiled=True).reshape(-1)
    projected = [part.astype(jnp.float32) for part in split_rows(proj_mine, row_shapes)]
    results = [
        adam_moments(first, second, proj) for first, second, proj in zip(firsts, seconds, projected)
    ]
    dir_all = jnp.concatenate([result[2].reshape(-1) for result in results])
    dir_gathered = lax.all_gather(dir_all, "tensor", axis=0, tiled=False)
    directions = split_rows(dir_gathered, row_shapes)
    outputs = []
    for weight, direction, basis, result in zip(weights, directions, bases, results):
        count, rows, cols = weight.shape
        update = jnp.einsum("jsmr,scr->sjmc", direction, basis, preferred_element_type=jnp.float32)
        update = update.reshape(count, rows, cols)
        weight_new = (0.99 * weight.astype(jnp.float32) - 2.0 * update).astype(jnp.bfloat16)
        outputs.append((weight_new, result[0], result[1]))
    return (
        outputs[0][0],
        outputs[0][1],
        outputs[0][2],
        outputs[1][0],
        outputs[1][1],
        outputs[1][2],
        outputs[2][0],
        outputs[2][1],
        outputs[2][2],
    )


def solution(mesh):
    in_specs = (
        P(None, "shard", "tensor"),
        P(None, "shard", "tensor"),
        P(None, ("shard", "tensor"), None),
        P(None, ("shard", "tensor"), None),
        P(None, "tensor", None),
        P(None, "shard", "tensor"),
        P(None, "shard", "tensor"),
        P(None, ("shard", "tensor"), None),
        P(None, ("shard", "tensor"), None),
        P(None, "tensor", None),
        P(None, "shard", "tensor"),
        P(None, "shard", "tensor"),
        P(None, ("shard", "tensor"), None),
        P(None, ("shard", "tensor"), None),
        P(None, "tensor", None),
    )
    out_specs = (
        P(None, "shard", "tensor"),
        P(None, ("shard", "tensor"), None),
        P(None, ("shard", "tensor"), None),
        P(None, "shard", "tensor"),
        P(None, ("shard", "tensor"), None),
        P(None, ("shard", "tensor"), None),
        P(None, "shard", "tensor"),
        P(None, ("shard", "tensor"), None),
        P(None, ("shard", "tensor"), None),
    )
    return jax.shard_map(
        functools.partial(per_device, mesh.shape["tensor"]), mesh=mesh, in_specs=in_specs, out_specs=out_specs, check_vma=False
    )
```

```python
import functools

import jax
import jax.numpy as jnp
from jax import lax
from jax.experimental import pallas as pl
from jax.sharding import PartitionSpec as P

NS_ITERS = 3


HIGHEST = lax.Precision.HIGHEST
HIGH = lax.Precision.HIGH


def local_gram(back):
    return jnp.einsum("sdk,sdl->skl", back, back, preferred_element_type=jnp.float32)


def symmetric_psum(gram, axis):
    half = gram.shape[1] // 2
    top, corner = lax.psum((gram[:, :half, :], gram[:, half:, half:]), axis)
    bottom = jnp.concatenate([jnp.swapaxes(top[:, :, half:], 1, 2), corner], axis=2)
    return jnp.concatenate([top, bottom], axis=1)


def polish_small(back, gram):
    trace = jnp.einsum("skk->s", gram)
    scale = 1.0 / jnp.sqrt(trace + 1e-06)
    small = gram * (scale * scale)[:, None, None]
    rank = gram.shape[1]
    eye = jnp.eye(rank, dtype=jnp.float32)[None, :, :]
    factor = None
    for step in range(NS_ITERS):
        square = jnp.einsum("skl,slm->skm", small, small, precision=HIGH)
        turn = 3.4445 * eye - 4.775 * small + 2.0315 * square
        if factor is None:
            factor = turn
        else:
            factor = jnp.einsum("skl,slm->skm", factor, turn, precision=HIGH)
        if step + 1 < NS_ITERS:
            small = jnp.einsum(
                "skl,slm->skm",
                turn,
                jnp.einsum("skl,slm->skm", small, turn, precision=HIGH),
                precision=HIGH,
            )
    return apply_polish(back, factor, scale)


def polish_kernel(back_ref, factor_ref, scale_ref, out_ref):
    back = back_ref[0]
    factor = factor_ref[0]
    high = factor.astype(jnp.bfloat16)
    low = (factor - high.astype(jnp.float32)).astype(jnp.bfloat16)
    polished = jnp.dot(back, high, preferred_element_type=jnp.float32)
    polished = polished + jnp.dot(back, low, preferred_element_type=jnp.float32)
    out_ref[0] = (polished * scale_ref[0, 0:1, 0:1]).astype(out_ref.dtype)


def apply_polish(back, factor, scale):
    count, rows, rank = back.shape
    scales = jnp.broadcast_to(scale[:, None, None], (count, 8, 128))
    return pl.pallas_call(
        polish_kernel,
        grid=(count,),
        in_specs=[
            pl.BlockSpec((1, rows, rank), lambda s: (s, 0, 0)),
            pl.BlockSpec((1, rank, rank), lambda s: (s, 0, 0)),
            pl.BlockSpec((1, 8, 128), lambda s: (s, 0, 0)),
        ],
        out_specs=pl.BlockSpec((1, rows, rank), lambda s: (s, 0, 0)),
        out_shape=jax.ShapeDtypeStruct(back.shape, jnp.bfloat16),
        cost_estimate=pl.CostEstimate(
            flops=4 * count * rows * rank * rank,
            bytes_accessed=4 * count * rows * rank + 4 * count * rank * rank,
            transcendentals=0,
        ),
    )(back, factor, scales)


def update_kernel(parts, part_rows, direction_ref, basis_ref, weight_ref, out_ref):
    for part in range(parts):
        rows = pl.ds(part * part_rows, part_rows)
        update = lax.dot_general(
            direction_ref[part],
            basis_ref[0],
            (((1,), (1,)), ((), ())),
            preferred_element_type=jnp.float32,
        )
        weight = weight_ref[0, rows, :].astype(jnp.float32)
        out_ref[0, rows, :] = (0.99 * weight + update).astype(out_ref.dtype)


def row_block(rows):
    for block in (1024, 1000, 800, 512, 500, 400, 256, 200, 128, 64, 32, 16, 8):
        if rows % block == 0:
            return block
    return rows


def aligned(part_rows):
    return part_rows % 8 == 0


def apply_update(gathered, offset, part_rows, basis, weight):
    count, rows, cols = weight.shape
    tensor_size, _, rank = gathered.shape
    if aligned(part_rows):
        parts = tensor_size if tensor_size * part_rows <= 1024 else 1
        grid = (count, tensor_size // parts)
        first = offset // part_rows
        direction = gathered
        direction_spec = pl.BlockSpec(
            (parts, part_rows, rank), lambda s, i: (i, first + s, 0)
        )
        block = parts * part_rows
    else:
        piece = gathered[:, offset:offset + count * part_rows]
        piece = piece.reshape(tensor_size, count, part_rows, rank)
        direction = jnp.moveaxis(piece, 0, 1).reshape(count, rows, rank)
        parts = 1
        block = row_block(rows)
        part_rows = block
        grid = (count, rows // block)
        direction_spec = pl.BlockSpec((1, block, rank), lambda s, i: (s, i, 0))
    return pl.pallas_call(
        functools.partial(update_kernel, parts, part_rows),
        grid=grid,
        in_specs=[
            direction_spec,
            pl.BlockSpec((1, cols, rank), lambda s, i: (s, 0, 0)),
            pl.BlockSpec((1, block, cols), lambda s, i: (s, i, 0)),
        ],
        out_specs=pl.BlockSpec((1, block, cols), lambda s, i: (s, i, 0)),
        out_shape=jax.ShapeDtypeStruct(weight.shape, weight.dtype),
        cost_estimate=pl.CostEstimate(
            flops=2 * count * rows * cols * rank,
            bytes_accessed=4 * count * rows * cols + 2 * count * (rows + cols) * rank,
            transcendentals=0,
        ),
    )(direction, basis, weight)


def adam_moments(first, second, projected):
    first_new = 0.9 * first + 0.1 * projected
    second_new = 0.999 * second + 0.001 * projected * projected
    direction = first_new / (1.0 - 0.9**10) / (jnp.sqrt(second_new / (1.0 - 0.999**10)) + 1e-08)
    return (first_new, second_new, (-2.0 * direction).astype(jnp.bfloat16))


def split_rows(flat, shapes):
    parts = []
    offset = 0
    for shape in shapes:
        size = 1
        for dim in shape:
            size *= dim
        parts.append(flat[..., offset:offset + size].reshape(flat.shape[:-1] + shape))
        offset += size
    return parts


def refresh(tensor_size, groups):
    weights = [group[0] for group in groups]
    grads = [group[1] for group in groups]
    firsts = [group[2] for group in groups]
    seconds = [group[3] for group in groups]
    olds = [group[4] for group in groups]
    counts = [grad.shape[0] for grad in grads]
    sketch_terms = [
        jnp.einsum("smc,scr->smr", grad, old, preferred_element_type=jnp.float32).astype(jnp.bfloat16)
        for grad, old in zip(grads, olds)
    ]
    sketches = lax.psum(tuple(sketch_terms), "tensor")
    back_terms = [
        jnp.einsum("smc,smr->scr", grad, sketch, preferred_element_type=jnp.float32)
        for grad, sketch in zip(grads, sketches)
    ]
    back_all = jnp.concatenate(back_terms, axis=0).astype(jnp.bfloat16)
    backs = lax.psum(back_all, "shard")
    grams = symmetric_psum(local_gram(backs), "tensor")
    basis_all = polish_small(backs, grams)
    bases = []
    offset = 0
    for count in counts:
        bases.append(basis_all[offset:offset + count])
        offset += count
    proj_parts = []
    row_shapes = []
    for grad, basis in zip(grads, bases):
        count, rows, cols = grad.shape
        split = grad.reshape(count, tensor_size, rows // tensor_size, cols)
        proj = jnp.einsum("sjmc,scr->jsmr", split, basis, preferred_element_type=jnp.float32)
        row_shapes.append((count, rows // tensor_size, basis.shape[2]))
        proj_parts.append(proj.reshape(tensor_size, -1, basis.shape[2]).astype(jnp.bfloat16))
    proj_all = jnp.concatenate(proj_parts, axis=1)
    proj_mine = lax.psum_scatter(proj_all, "tensor", scatter_dimension=0, tiled=True).reshape(-1)
    projected = [part.astype(jnp.float32) for part in split_rows(proj_mine, row_shapes)]
    results = [
        adam_moments(first, second, proj) for first, second, proj in zip(firsts, seconds, projected)
    ]
    order = sorted(range(len(results)), key=lambda index: -row_shapes[index][1])
    offsets = [0] * len(results)
    pieces = []
    cursor = 0
    for index in order:
        count, part_rows, rank = row_shapes[index]
        start = cursor
        if aligned(part_rows):
            start = -(-cursor // part_rows) * part_rows
        if start > cursor:
            pieces.append(jnp.zeros((start - cursor, rank), jnp.bfloat16))
        pieces.append(results[index][2].reshape(count * part_rows, rank))
        offsets[index] = start
        cursor = start + count * part_rows
    dir_all = jnp.concatenate(pieces, axis=0)
    gathered = lax.all_gather(dir_all, "tensor", axis=0, tiled=False)
    outputs = []
    for index, (weight, basis, result) in enumerate(zip(weights, bases, results)):
        part_rows = row_shapes[index][1]
        weight_new = apply_update(gathered, offsets[index], part_rows, basis, weight)
        outputs.append((weight_new, result[0], result[1]))
    return outputs


def per_device(tensor_size, *arrays):
    wide, narrow, vocab = arrays[0:5], arrays[5:10], arrays[10:15]
    wide_out, narrow_out, vocab_out = refresh(tensor_size, [wide, narrow, vocab])
    return tuple(wide_out) + tuple(narrow_out) + tuple(vocab_out)


def solution(mesh):
    in_specs = (
        P(None, "shard", "tensor"),
        P(None, "shard", "tensor"),
        P(None, ("shard", "tensor"), None),
        P(None, ("shard", "tensor"), None),
        P(None, "tensor", None),
        P(None, "shard", "tensor"),
        P(None, "shard", "tensor"),
        P(None, ("shard", "tensor"), None),
        P(None, ("shard", "tensor"), None),
        P(None, "tensor", None),
        P(None, "shard", "tensor"),
        P(None, "shard", "tensor"),
        P(None, ("shard", "tensor"), None),
        P(None, ("shard", "tensor"), None),
        P(None, "tensor", None),
    )
    out_specs = (
        P(None, "shard", "tensor"),
        P(None, ("shard", "tensor"), None),
        P(None, ("shard", "tensor"), None),
        P(None, "shard", "tensor"),
        P(None, ("shard", "tensor"), None),
        P(None, ("shard", "tensor"), None),
        P(None, "shard", "tensor"),
        P(None, ("shard", "tensor"), None),
        P(None, ("shard", "tensor"), None),
    )
    return jax.shard_map(
        functools.partial(per_device, mesh.shape["tensor"]), mesh=mesh, in_specs=in_specs, out_specs=out_specs, check_vma=False
    )
```
